512 devices in a mesh: band: 16 (over y, core), dom: 32 (over z, x).
Axes of the slice: x: 4, y: 8, z: 8, core: 2. Of those that a mesh axis runs over, the one named last changes fastest.
Arguments:
- orbitals: float32 [32, 2, 256, 8, 128], P('band', None, 'dom'), may hold values from -6 to 6
- ace_vectors: float32 [16, 2, 256, 8, 128], P(None, None, 'dom'), may hold values from -0.078125 to 0.078125
- local_potential: float32 [256, 8, 128], P('dom'), may hold values from -1 to 1
- field_strength: float32 [2], replicated, may hold values from -2 to 2
- run_projectors: float32 [1024, 4, 256], P('dom'), may hold values from -0.09375 to 0.09375
- run_atom: int32 [1024], P('dom'), may hold values from 0 to 127, as said below
- run_count: int32 [1024], P('dom'), may hold values from 1 to 256, as said below
- run_start: int32 [1024], P('dom'), may hold values from 0 to 7936, as said below
- kb_energy: float32 [128], P('dom'), may hold values from 0.1 to 1
Outputs:
- propagated: float32 [32, 2, 256, 8, 128], P('band', None, 'dom')
- forces: float32 [2, 3, 128], P(None, None, 'dom')
The draws below stay inside these ranges and needn't reach their ends.
Inputs may be any that keep to these rules, and one draw needn't show every extreme that they name: `run_atom`: atom a is owned by index a // 4 of dom. The 32 runs of one dom index name atoms of any one owner at most 2 times, and exactly 2 times for some owner. `run_count`: every dom index has a run of 256 points. `run_start`: every dom index has a run that starts at cell 8192 - 256.
All inputs are finite; a program needn't handle non-finite values.
Results may differ from the reference program's by a relative error of at most 0.0003.
Values sent between devices are 32-bit elements; how exact they have to be, the bound alone decides.
No kernel may reach another device: no remote copies, remote signals or barrier semaphores. Data moves between devices by JAX's collectives and lax.ppermute only.
A program may use at most 64 MiB of HBM per device.

```python
import math
import jax
import jax.numpy as jnp
from jax import lax

ORB_DEV = 2
NACE = 16
NX = 8
NY = 128
PTS = 256
SLOTS = 32
ATOM_DEV = 4
STEPS = 2
TAYLOR = 4
ORBS = 32
NZ = 256
CELLS = 8192
SLOTS_ALL = 1024
CAP = 2
ATOMS = 128
N_BAND = 16


def draw_run_atom(key, part):
    dom_count = SLOTS_ALL // SLOTS

    def domain_runs(key_domain):
        key_crowd, key_order, key_local, key_shuffle = jax.random.split(key_domain, 4)
        crowded = jax.random.randint(key_crowd, (), 0, dom_count)
        tickets = jnp.arange((dom_count - 1) * CAP, dtype=jnp.int32) // CAP
        shuffled = jax.random.permutation(key_order, (dom_count - 1) * CAP)
        others = (crowded + 1 + tickets[shuffled][:SLOTS - CAP]) % dom_count
        owners = jnp.concatenate([jnp.full((CAP,), crowded, jnp.int32), others.astype(jnp.int32)])
        owners = owners[jax.random.permutation(key_shuffle, SLOTS)]
        local_ids = jax.random.randint(key_local, (SLOTS,), 0, ATOM_DEV)
        return (owners * ATOM_DEV + local_ids).astype(jnp.int32)
    key_list = jax.random.split(jax.random.fold_in(key, 11), dom_count)
    return jax.vmap(domain_runs)(key_list).reshape(-1).astype(jnp.int32)


def draw_run_count(key, part):
    dom_count = SLOTS_ALL // SLOTS
    key_counts, key_place = jax.random.split(jax.random.fold_in(key, 12))
    counts = jax.random.randint(key_counts, (dom_count, SLOTS), 1, PTS + 1)
    full_slot = jax.random.randint(key_place, (dom_count, 1), 0, SLOTS)
    counts = jnp.where(jnp.arange(SLOTS)[None, :] == full_slot, PTS, counts)
    return counts.reshape(-1).astype(jnp.int32)


def draw_run_start(key, part):
    dom_count = SLOTS_ALL // SLOTS
    key_starts, key_place = jax.random.split(jax.random.fold_in(key, 13))
    starts = jax.random.randint(key_starts, (dom_count, SLOTS), 0, CELLS - PTS + 1)
    last_slot = jax.random.randint(key_place, (dom_count, 1), 0, SLOTS)
    starts = jnp.where(jnp.arange(SLOTS)[None, :] == last_slot, CELLS - PTS, starts)
    return starts.reshape(-1).astype(jnp.int32)


def block_scale(rng, shape, shards, least, high):
    def one(dim, shards_of):
        draws = jax.random.uniform(jax.random.fold_in(jax.random.fold_in(rng, 6), dim), (shards_of,), jnp.float32, least / len(shards), high / len(shards))
        return jnp.repeat(jnp.exp(draws), shape[dim] // shards_of).reshape((-1,) + (1,) * (len(shape) - dim - 1))

    gain = one(*shards[0])
    for cut in shards[1:]:
        gain = gain * one(*cut)
    return gain


def centred(stream_key, dims, width, limit, shards=(), held_as=jnp.bfloat16):
    result = jax.random.normal(stream_key, dims, jnp.float32) * width
    if len(shards) > 0:
        result = block_scale(stream_key, dims, shards, -0.22, 0.18) * result
    return jnp.clip(result, min=-limit, max=limit).astype(held_as)


def setup_inputs(seed: int = 0) -> dict:
    seeds = jax.random.split(jax.random.key(seed), 10)
    orbitals = centred(seeds[0], (ORBS, 2, NZ, NX, NY), 1.0, 6.0, ((0, 16), (2, 32)), jnp.float32)
    ace_vectors = centred(seeds[1], (NACE, 2, NZ, NX, NY), (NX * NY * NZ // 48) ** -0.5, 0.078125, ((2, 32),), jnp.float32)
    local_potential = jnp.clip(jax.random.uniform(seeds[2], (NZ, NX, NY), jnp.float32, -1.0, 1.0) * block_scale(seeds[2], (NZ, NX, NY), ((0, 32),), -0.4, 0.0), -1.0, 1.0)
    field_strength = jnp.clip(jax.random.uniform(seeds[3], (STEPS,), jnp.float32, -2.0, 2.0), -2.0, 2.0)
    run_projectors = centred(seeds[4], (SLOTS_ALL, 4, PTS), (PTS * 16) ** -0.5, 0.09375, ((0, 32),), jnp.float32)
    run_atom = draw_run_atom(jax.random.fold_in(seeds[9], 71), 0)
    run_count = draw_run_count(jax.random.fold_in(seeds[9], 71), 0)
    run_start = draw_run_start(jax.random.fold_in(seeds[9], 71), 0)
    kb_energy = jnp.clip(jnp.exp(math.log(1.0) - 2.3025851 * jax.random.uniform(seeds[8], (ATOMS,), jnp.float32) ** block_scale(seeds[8], (ATOMS,), ((0, 32),), -0.2, 0.2)), 0.1, 1.0)
    return {"orbitals": orbitals, "ace_vectors": ace_vectors, "local_potential": local_potential, "field_strength": field_strength, "run_projectors": run_projectors, "run_atom": run_atom, "run_count": run_count, "run_start": run_start, "kb_energy": kb_energy}


spacing = 0.5
time_step = 0.04
highest = lax.Precision.HIGHEST


def laplace(extended):
    middle = extended[:, :, 2:-2]
    along_z = 16.0 * (extended[:, :, 3:-1] + extended[:, :, 1:-3]) - (extended[:, :, 4:] + extended[:, :, :-4])
    along_x = 16.0 * (jnp.roll(middle, 1, 3) + jnp.roll(middle, -1, 3)) - (jnp.roll(middle, 2, 3) + jnp.roll(middle, -2, 3))
    along_y = 16.0 * (jnp.roll(middle, 1, 4) + jnp.roll(middle, -1, 4)) - (jnp.roll(middle, 2, 4) + jnp.roll(middle, -2, 4))
    return (along_z + along_x + along_y - 90.0 * middle) / (12.0 * spacing * spacing)


def projections(ace_rows, term):
    vector_count = ace_rows.shape[0]
    orbital_count = term.shape[0]
    products = lax.dot_general(ace_rows.reshape(vector_count * 2, -1), term.reshape(orbital_count * 2, -1),
                               (((1,), (1,)), ((), ())), precision=highest, preferred_element_type=jnp.float32)
    products = products.reshape(vector_count, 2, orbital_count, 2)
    return jnp.stack([products[:, 0, :, 0] + products[:, 1, :, 1], products[:, 0, :, 1] - products[:, 1, :, 0]])


def fock_term(ace_rows, weights):
    vector_count = ace_rows.shape[0]
    orbital_count = weights.shape[2]
    real_part = weights[0]
    imag_part = weights[1]
    coefficients = jnp.stack([jnp.stack([real_part, imag_part], axis=-1), jnp.stack([-imag_part, real_part], axis=-1)], axis=1)
    applied = lax.dot_general(coefficients.reshape(vector_count * 2, orbital_count * 2), ace_rows.reshape(vector_count * 2, -1),
                              (((0,), (0,)), ((), ())), precision=highest, preferred_element_type=jnp.float32)
    return applied.reshape((orbital_count, 2) + ace_rows.shape[2:])


def next_term(applied, degree):
    factor = time_step / degree
    return jnp.stack([factor * applied[:, 1], -factor * applied[:, 0]], axis=1)


def propagate(block, potential, ace_vectors):
    accumulated = block
    term = block
    for degree in range(1, TAYLOR + 1):
        extended = jnp.pad(term, ((0, 0), (0, 0), (2, 2), (0, 0), (0, 0)))
        applied = -0.5 * laplace(extended) + potential * term - fock_term(ace_vectors, projections(ace_vectors, term))
        term = next_term(applied, degree)
        accumulated = accumulated + term
    return accumulated


def atom_forces(flattened, run_projectors, run_atom, run_count, run_start, kb_energy):
    domain = jnp.arange(SLOTS_ALL, dtype=jnp.int32) // SLOTS
    run_offset = (domain * CELLS + run_start).astype(jnp.int32)

    def run_terms(run_item):
        run_begin, run_len, values = run_item
        piece = lax.dynamic_slice_in_dim(flattened, run_begin, PTS, 1)
        in_run = jnp.arange(PTS, dtype=jnp.int32) < run_len
        masked = jnp.where(in_run[None, :], values, 0.0)
        return lax.dot_general(masked, piece, (((1,), (1,)), ((), ())), precision=highest, preferred_element_type=jnp.float32)

    partials = lax.map(run_terms, (run_offset, run_count, run_projectors))
    totals = jax.ops.segment_sum(partials, run_atom, num_segments=ATOMS)
    return 2.0 * kb_energy[None, :] * jnp.einsum("ar,acr->ca", totals[:, 0], totals[:, 1:], precision=highest)


def reference(orbitals, ace_vectors, local_potential, field_strength, run_projectors, run_atom, run_count, run_start, kb_energy):
    blocks = orbitals.reshape(N_BAND, ORB_DEV, 2, NZ, NX, NY)
    height = 2.0 * (jnp.arange(NZ, dtype=jnp.float32) + 0.5) / NZ - 1.0
    results = []
    for step_index in range(STEPS):
        potential = local_potential + field_strength[step_index] * height[:, None, None]

        def advance(block):
            return propagate(block, potential, ace_vectors)

        blocks = lax.map(advance, blocks)
        results.append(atom_forces(blocks.reshape(ORBS * 2, NZ * NX * NY), run_projectors, run_atom, run_count, run_start, kb_energy))
    return blocks.reshape(ORBS, 2, NZ, NX, NY), jnp.stack(results)
```

```python
import jax
import jax.numpy as jnp
from jax import lax
from jax.sharding import PartitionSpec as P

STEPS = 2
TAYLOR = 4


spacing = 0.5
time_step = 0.04
highest = lax.Precision.HIGHEST


def extended_2(block, sides, width):
    for axis, dim in sides:
        count = lax.axis_size(axis)
        forward = [(i, i + 1) for i in range(count - 1)]
        backward = [(target, source) for source, target in forward]
        low = lax.ppermute(
            lax.slice_in_dim(block, block.shape[dim] - width, None, axis=dim), axis, forward
        )
        high = lax.ppermute(lax.slice_in_dim(block, 0, width, axis=dim), axis, backward)
        block = jnp.concatenate([low, block, high], axis=dim)
    return block


def laplace(extended):
    middle = extended[:, :, 2:-2]
    along_z = 16.0 * (extended[:, :, 3:-1] + extended[:, :, 1:-3]) - (
        extended[:, :, 4:] + extended[:, :, :-4]
    )
    along_x = 16.0 * (jnp.roll(middle, 1, 3) + jnp.roll(middle, -1, 3)) - (
        jnp.roll(middle, 2, 3) + jnp.roll(middle, -2, 3)
    )
    along_y = 16.0 * (jnp.roll(middle, 1, 4) + jnp.roll(middle, -1, 4)) - (
        jnp.roll(middle, 2, 4) + jnp.roll(middle, -2, 4)
    )
    return (along_z + along_x + along_y - 90.0 * middle) / (12.0 * spacing * spacing)


def projections(ace_rows, term):
    vector_count = ace_rows.shape[0]
    orbital_count = term.shape[0]
    products = lax.dot_general(
        ace_rows.reshape(vector_count * 2, -1),
        term.reshape(orbital_count * 2, -1),
        (((1,), (1,)), ((), ())),
        precision=highest,
        preferred_element_type=jnp.float32,
    )
    products = products.reshape(vector_count, 2, orbital_count, 2)
    return jnp.stack(
        [products[:, 0, :, 0] + products[:, 1, :, 1], products[:, 0, :, 1] - products[:, 1, :, 0]]
    )


def butterfly_sum(x, axis):
    count = lax.axis_size(axis)
    if count & (count - 1):
        return lax.psum(x, axis)
    step = 1
    while step < count:
        pairs = [(i, i ^ step) for i in range(count)]
        x = x + lax.ppermute(x, axis, pairs)
        step *= 2
    return x


def ace_weights(ace_rows, term):
    return butterfly_sum(projections(ace_rows, term), "dom")


def fock_term(ace_rows, weights):
    vector_count = ace_rows.shape[0]
    orbital_count = weights.shape[2]
    real_part = weights[0]
    imag_part = weights[1]
    coefficients = jnp.stack(
        [jnp.stack([real_part, imag_part], axis=-1), jnp.stack([-imag_part, real_part], axis=-1)],
        axis=1,
    )
    applied = lax.dot_general(
        coefficients.reshape(vector_count * 2, orbital_count * 2),
        ace_rows.reshape(vector_count * 2, -1),
        (((0,), (0,)), ((), ())),
        precision=highest,
        preferred_element_type=jnp.float32,
    )
    return applied.reshape((orbital_count, 2) + ace_rows.shape[2:])


def next_term(applied, degree):
    factor = time_step / degree
    return jnp.stack([factor * applied[:, 1], -factor * applied[:, 0]], axis=1)


def taylor_rounds(current, potential, ace_vectors):
    accumulated = current
    term = current
    for degree in range(1, TAYLOR + 1):
        extended = extended_2(term, (("dom", 2),), 2)
        weights = ace_weights(ace_vectors, term)
        applied = -0.5 * laplace(extended) + potential * term - fock_term(ace_vectors, weights)
        term = next_term(applied, degree)
        accumulated = accumulated + term
    return accumulated


def atom_partials(current, run_projectors, run_atom, run_count, run_start, kb_energy):
    row_count = current.shape[0] * 2
    point_count = run_projectors.shape[2]
    atom_dev = kb_energy.shape[0]
    dom_count = lax.axis_size("dom")
    slot_count = run_atom.shape[0]
    flattened = current.reshape(row_count, -1)

    def cut_run(run_begin):
        return lax.dynamic_slice_in_dim(flattened, run_begin, point_count, 1)

    pieces = jax.vmap(cut_run)(run_start)
    in_run = jnp.arange(point_count, dtype=jnp.int32)[None, :] < run_count[:, None]
    masked = jnp.where(in_run[:, None, :], run_projectors, 0.0)
    partials = jnp.einsum("scp,srp->scr", masked, pieces, precision=highest)
    capacity = 2 * slot_count // dom_count
    owner = run_atom // atom_dev
    slot_ids = jnp.arange(slot_count, dtype=jnp.int32)
    same_owner = (owner[:, None] == owner[None, :]) & (slot_ids[None, :] < slot_ids[:, None])
    owner_rank = jnp.sum(same_owner.astype(jnp.int32), axis=1)
    slot_pos = owner * capacity + owner_rank
    placement = jnp.arange(dom_count * capacity, dtype=jnp.int32)[:, None] == slot_pos[None, :]
    outgoing = jnp.einsum("ks,scr->kcr", placement.astype(jnp.float32), partials, precision=highest)
    atom_slots = jnp.max(jnp.where(placement, (run_atom % atom_dev)[None, :], -1), axis=1)
    received, received_ids = (
        lax.all_to_all(outgoing, "dom", split_axis=0, concat_axis=0, tiled=True),
        lax.all_to_all(atom_slots, "dom", split_axis=0, concat_axis=0, tiled=True),
    )
    matches = (received_ids[None, :] == jnp.arange(atom_dev, dtype=jnp.int32)[:, None]).astype(
        jnp.float32
    )
    atom_totals = jnp.einsum("ak,kcr->acr", matches, received, precision=highest)
    return (
        2.0
        * kb_energy[None, :]
        * jnp.einsum("ar,acr->ca", atom_totals[:, 0], atom_totals[:, 1:], precision=highest)
    )


def shards(
    orbitals,
    ace_vectors,
    local_potential,
    field_strength,
    run_projectors,
    run_atom,
    run_count,
    run_start,
    kb_energy,
):
    plane_count = orbitals.shape[2]
    plane_total = plane_count * lax.axis_size("dom")
    first_plane = lax.axis_index("dom") * plane_count
    height = (
        2.0
        * ((first_plane + jnp.arange(plane_count, dtype=jnp.int32)).astype(jnp.float32) + 0.5)
        / plane_total
        - 1.0
    )
    current = orbitals
    results = []
    for step_index in range(STEPS):
        strength = field_strength[step_index]
        current = taylor_rounds(
            current, local_potential + strength * height[:, None, None], ace_vectors
        )
        partial_force = atom_partials(
            current, run_projectors, run_atom, run_count, run_start, kb_energy
        )
        partial_force = lax.psum(partial_force, "band")
        results.append(partial_force)
    forces = jnp.stack(results)
    return (current, forces)


def solution(mesh):
    in_specs = (
        P("band", None, "dom", None, None),
        P(None, None, "dom", None, None),
        P("dom", None, None),
        P(),
        P("dom", None, None),
        P("dom"),
        P("dom"),
        P("dom"),
        P("dom"),
    )
    out_specs = (P("band", None, "dom", None, None), P(None, None, "dom"))
    return jax.shard_map(shards, mesh=mesh, in_specs=in_specs, out_specs=out_specs, check_vma=False)
```

```python
import jax
import jax.numpy as jnp
from jax import lax
from jax.sharding import PartitionSpec as P

STEPS = 2
TAYLOR = 4


spacing = 0.5
time_step = 0.04
highest = lax.Precision.HIGHEST


def extended_2(block, sides, width):
    for axis, dim in sides:
        count = lax.axis_size(axis)
        forward = [(i, i + 1) for i in range(count - 1)]
        backward = [(target, source) for source, target in forward]
        low = lax.ppermute(
            lax.slice_in_dim(block, block.shape[dim] - width, None, axis=dim), axis, forward
        )
        high = lax.ppermute(lax.slice_in_dim(block, 0, width, axis=dim), axis, backward)
        block = jnp.concatenate([low, block, high], axis=dim)
    return block


def laplace(extended):
    middle = extended[:, :, 2:-2]
    along_z = 16.0 * (extended[:, :, 3:-1] + extended[:, :, 1:-3]) - (
        extended[:, :, 4:] + extended[:, :, :-4]
    )
    along_x = 16.0 * (jnp.roll(middle, 1, 3) + jnp.roll(middle, -1, 3)) - (
        jnp.roll(middle, 2, 3) + jnp.roll(middle, -2, 3)
    )
    along_y = 16.0 * (jnp.roll(middle, 1, 4) + jnp.roll(middle, -1, 4)) - (
        jnp.roll(middle, 2, 4) + jnp.roll(middle, -2, 4)
    )
    return (along_z + along_x + along_y - 90.0 * middle) / (12.0 * spacing * spacing)


def projections(ace_rows, term):
    vector_count = ace_rows.shape[0]
    orbital_count = term.shape[0]
    products = lax.dot_general(
        ace_rows.reshape(vector_count * 2, -1),
        term.reshape(orbital_count * 2, -1),
        (((1,), (1,)), ((), ())),
        precision=highest,
        preferred_element_type=jnp.float32,
    )
    products = products.reshape(vector_count, 2, orbital_count, 2)
    return jnp.stack(
        [products[:, 0, :, 0] + products[:, 1, :, 1], products[:, 0, :, 1] - products[:, 1, :, 0]]
    )


def exchange_sum(x, axis):
    count = lax.axis_size(axis)
    copies = jnp.broadcast_to(x[None], (count,) + x.shape)
    return jnp.sum(lax.all_to_all(copies, axis, 0, 0, tiled=False), axis=0)


def ace_weights(ace_rows, term):
    return exchange_sum(projections(ace_rows, term), "dom")


def fock_term(ace_rows, weights):
    vector_count = ace_rows.shape[0]
    orbital_count = weights.shape[2]
    real_part = weights[0]
    imag_part = weights[1]
    coefficients = jnp.stack(
        [jnp.stack([real_part, imag_part], axis=-1), jnp.stack([-imag_part, real_part], axis=-1)],
        axis=1,
    )
    applied = lax.dot_general(
        coefficients.reshape(vector_count * 2, orbital_count * 2),
        ace_rows.reshape(vector_count * 2, -1),
        (((0,), (0,)), ((), ())),
        precision=highest,
        preferred_element_type=jnp.float32,
    )
    return applied.reshape((orbital_count, 2) + ace_rows.shape[2:])


def next_term(applied, degree):
    factor = time_step / degree
    return jnp.stack([factor * applied[:, 1], -factor * applied[:, 0]], axis=1)


def taylor_rounds(current, potential, ace_vectors):
    accumulated = current
    term = current
    for degree in range(1, TAYLOR + 1):
        extended = extended_2(term, (("dom", 2),), 2)
        weights = ace_weights(ace_vectors, term)
        applied = -0.5 * laplace(extended) + potential * term - fock_term(ace_vectors, weights)
        term = next_term(applied, degree)
        accumulated = accumulated + term
    return accumulated


def atom_partials(current, run_projectors, run_atom, run_count, run_start, kb_energy):
    row_count = current.shape[0] * 2
    point_count = run_projectors.shape[2]
    atom_dev = kb_energy.shape[0]
    dom_count = lax.axis_size("dom")
    slot_count = run_atom.shape[0]
    flattened = current.reshape(row_count, -1)

    def cut_run(run_begin):
        return lax.dynamic_slice_in_dim(flattened, run_begin, point_count, 1)

    pieces = jax.vmap(cut_run)(run_start)
    in_run = jnp.arange(point_count, dtype=jnp.int32)[None, :] < run_count[:, None]
    masked = jnp.where(in_run[:, None, :], run_projectors, 0.0)
    partials = jnp.einsum("scp,srp->scr", masked, pieces, precision=highest)
    capacity = 2 * slot_count // dom_count
    owner = run_atom // atom_dev
    slot_ids = jnp.arange(slot_count, dtype=jnp.int32)
    same_owner = (owner[:, None] == owner[None, :]) & (slot_ids[None, :] < slot_ids[:, None])
    owner_rank = jnp.sum(same_owner.astype(jnp.int32), axis=1)
    slot_pos = owner * capacity + owner_rank
    placement = jnp.arange(dom_count * capacity, dtype=jnp.int32)[:, None] == slot_pos[None, :]
    outgoing = jnp.einsum("ks,scr->kcr", placement.astype(jnp.float32), partials, precision=highest)
    atom_slots = jnp.max(jnp.where(placement, (run_atom % atom_dev)[None, :], -1), axis=1)
    received, received_ids = (
        lax.all_to_all(outgoing, "dom", split_axis=0, concat_axis=0, tiled=True),
        lax.all_to_all(atom_slots, "dom", split_axis=0, concat_axis=0, tiled=True),
    )
    matches = (received_ids[None, :] == jnp.arange(atom_dev, dtype=jnp.int32)[:, None]).astype(
        jnp.float32
    )
    atom_totals = jnp.einsum("ak,kcr->acr", matches, received, precision=highest)
    return (
        2.0
        * kb_energy[None, :]
        * jnp.einsum("ar,acr->ca", atom_totals[:, 0], atom_totals[:, 1:], precision=highest)
    )


def shards(
    orbitals,
    ace_vectors,
    local_potential,
    field_strength,
    run_projectors,
    run_atom,
    run_count,
    run_start,
    kb_energy,
):
    plane_count = orbitals.shape[2]
    plane_total = plane_count * lax.axis_size("dom")
    first_plane = lax.axis_index("dom") * plane_count
    height = (
        2.0
        * ((first_plane + jnp.arange(plane_count, dtype=jnp.int32)).astype(jnp.float32) + 0.5)
        / plane_total
        - 1.0
    )
    current = orbitals
    results = []
    for step_index in range(STEPS):
        strength = field_strength[step_index]
        current = taylor_rounds(
            current, local_potential + strength * height[:, None, None], ace_vectors
        )
        partial_force = atom_partials(
            current, run_projectors, run_atom, run_count, run_start, kb_energy
        )
        partial_force = lax.psum(partial_force, "band")
        results.append(partial_force)
    forces = jnp.stack(results)
    return (current, forces)


def solution(mesh):
    in_specs = (
        P("band", None, "dom", None, None),
        P(None, None, "dom", None, None),
        P("dom", None, None),
        P(),
        P("dom", None, None),
        P("dom"),
        P("dom"),
        P("dom"),
        P("dom"),
    )
    out_specs = (P("band", None, "dom", None, None), P(None, None, "dom"))
    return jax.shard_map(shards, mesh=mesh, in_specs=in_specs, out_specs=out_specs, check_vma=False)
```

```python
import jax
import jax.numpy as jnp
from jax import lax
from jax.sharding import PartitionSpec as P

STEPS = 2
TAYLOR = 4


spacing = 0.5
time_step = 0.04
highest = lax.Precision.HIGHEST


def extended_2(block, sides, width):
    for axis, dim in sides:
        count = lax.axis_size(axis)
        forward = [(i, i + 1) for i in range(count - 1)]
        backward = [(target, source) for source, target in forward]
        low = lax.ppermute(
            lax.slice_in_dim(block, block.shape[dim] - width, None, axis=dim), axis, forward
        )
        high = lax.ppermute(lax.slice_in_dim(block, 0, width, axis=dim), axis, backward)
        block = jnp.concatenate([low, block, high], axis=dim)
    return block


def laplace(extended):
    middle = extended[:, :, 2:-2]
    along_z = 16.0 * (extended[:, :, 3:-1] + extended[:, :, 1:-3]) - (
        extended[:, :, 4:] + extended[:, :, :-4]
    )
    along_x = 16.0 * (jnp.roll(middle, 1, 3) + jnp.roll(middle, -1, 3)) - (
        jnp.roll(middle, 2, 3) + jnp.roll(middle, -2, 3)
    )
    along_y = 16.0 * (jnp.roll(middle, 1, 4) + jnp.roll(middle, -1, 4)) - (
        jnp.roll(middle, 2, 4) + jnp.roll(middle, -2, 4)
    )
    return (along_z + along_x + along_y - 90.0 * middle) / (12.0 * spacing * spacing)


def projections(ace_rows, term):
    vector_count = ace_rows.shape[0]
    orbital_count = term.shape[0]
    products = lax.dot_general(
        ace_rows.reshape(vector_count * 2, -1),
        term.reshape(orbital_count * 2, -1),
        (((1,), (1,)), ((), ())),
        precision=highest,
        preferred_element_type=jnp.float32,
    )
    products = products.reshape(vector_count, 2, orbital_count, 2)
    return jnp.stack(
        [products[:, 0, :, 0] + products[:, 1, :, 1], products[:, 0, :, 1] - products[:, 1, :, 0]]
    )


def exchange_sum(x, axis):
    count = lax.axis_size(axis)
    copies = jnp.broadcast_to(x[None], (count,) + x.shape)
    return jnp.sum(lax.all_to_all(copies, axis, 0, 0, tiled=False), axis=0)


def ace_weights(ace_rows, term):
    return exchange_sum(projections(ace_rows, term), "dom")


def fock_term(ace_rows, weights):
    vector_count = ace_rows.shape[0]
    orbital_count = weights.shape[2]
    real_part = weights[0]
    imag_part = weights[1]
    coefficients = jnp.stack(
        [jnp.stack([real_part, imag_part], axis=-1), jnp.stack([-imag_part, real_part], axis=-1)],
        axis=1,
    )
    applied = lax.dot_general(
        coefficients.reshape(vector_count * 2, orbital_count * 2),
        ace_rows.reshape(vector_count * 2, -1),
        (((0,), (0,)), ((), ())),
        precision=highest,
        preferred_element_type=jnp.float32,
    )
    return applied.reshape((orbital_count, 2) + ace_rows.shape[2:])


def next_term(applied, degree):
    factor = time_step / degree
    return jnp.stack([factor * applied[:, 1], -factor * applied[:, 0]], axis=1)


def taylor_rounds(current, potential, ace_vectors):
    accumulated = current
    term = current
    for degree in range(1, TAYLOR + 1):
        extended = extended_2(term, (("dom", 2),), 2)
        weights = ace_weights(ace_vectors, term)
        applied = -0.5 * laplace(extended) + potential * term - fock_term(ace_vectors, weights)
        term = next_term(applied, degree)
        accumulated = accumulated + term
    return accumulated


def projector_matrix(run_projectors, run_count, run_start, cell_count):
    slot_count, comp_count, point_count = run_projectors.shape
    lanes = 128
    tiles_out = cell_count // lanes
    span = point_count // lanes + 1
    points = jnp.arange(point_count, dtype=jnp.int32)
    masked = jnp.where(points[None, None, :] < run_count[:, None, None], run_projectors, 0.0)
    window = jnp.pad(masked, ((0, 0), (0, 0), (0, span * lanes - point_count)))
    shift = run_start % lanes
    amount = 1
    while amount < lanes:
        moved = jnp.pad(window[:, :, : window.shape[2] - amount], ((0, 0), (0, 0), (amount, 0)))
        window = jnp.where(((shift // amount) % 2 == 1)[:, None, None], moved, window)
        amount *= 2
    window = window.reshape(slot_count, comp_count, span, lanes)
    first_tile = run_start // lanes
    tile_ids = jnp.arange(tiles_out, dtype=jnp.int32)
    full = jnp.zeros((slot_count, comp_count, tiles_out, lanes), jnp.float32)
    for offset in range(span):
        hit = (tile_ids[None, :] == (first_tile + offset)[:, None])[:, None, :, None]
        full = full + jnp.where(hit, window[:, :, offset][:, :, None, :], 0.0)
    return full.reshape(slot_count * comp_count, cell_count)


def run_partials(current, matrix, slot_count):
    flattened = current.reshape(current.shape[0] * 2, -1)
    products = jnp.einsum("kn,rn->kr", matrix, flattened, precision=highest)
    return products.reshape(slot_count, -1, flattened.shape[0])


def atom_forces(partials, run_atom, kb_energy):
    atom_dev = kb_energy.shape[0]
    dom_count = lax.axis_size("dom")
    slot_count = run_atom.shape[0]
    capacity = 2 * slot_count // dom_count
    owner = run_atom // atom_dev
    slot_ids = jnp.arange(slot_count, dtype=jnp.int32)
    same_owner = (owner[:, None] == owner[None, :]) & (slot_ids[None, :] < slot_ids[:, None])
    owner_rank = jnp.sum(same_owner.astype(jnp.int32), axis=1)
    slot_pos = owner * capacity + owner_rank
    placement = jnp.arange(dom_count * capacity, dtype=jnp.int32)[:, None] == slot_pos[None, :]
    outgoing = jnp.einsum("ks,stcr->ktcr", placement.astype(jnp.float32), partials, precision=highest)
    atom_slots = jnp.max(jnp.where(placement, (run_atom % atom_dev)[None, :], -1), axis=1)
    received, received_ids = (
        lax.all_to_all(outgoing, "dom", split_axis=0, concat_axis=0, tiled=True),
        lax.all_to_all(atom_slots, "dom", split_axis=0, concat_axis=0, tiled=True),
    )
    matches = (received_ids[None, :] == jnp.arange(atom_dev, dtype=jnp.int32)[:, None]).astype(
        jnp.float32
    )
    atom_totals = jnp.einsum("ak,ktcr->atcr", matches, received, precision=highest)
    return (
        2.0
        * kb_energy[None, None, :]
        * jnp.einsum("atr,atcr->tca", atom_totals[:, :, 0], atom_totals[:, :, 1:], precision=highest)
    )


def shards(
    orbitals,
    ace_vectors,
    local_potential,
    field_strength,
    run_projectors,
    run_atom,
    run_count,
    run_start,
    kb_energy,
):
    plane_count = orbitals.shape[2]
    plane_total = plane_count * lax.axis_size("dom")
    first_plane = lax.axis_index("dom") * plane_count
    height = (
        2.0
        * ((first_plane + jnp.arange(plane_count, dtype=jnp.int32)).astype(jnp.float32) + 0.5)
        / plane_total
        - 1.0
    )
    slot_count = run_projectors.shape[0]
    cell_count = orbitals[0, 0].size
    matrix = projector_matrix(run_projectors, run_count, run_start, cell_count)
    current = orbitals
    results = []
    for step_index in range(STEPS):
        strength = field_strength[step_index]
        current = taylor_rounds(
            current, local_potential + strength * height[:, None, None], ace_vectors
        )
        results.append(run_partials(current, matrix, slot_count))
    partials = jnp.stack(results, axis=1)
    forces = exchange_sum(atom_forces(partials, run_atom, kb_energy), "band")
    return (current, forces)


def solution(mesh):
    in_specs = (
        P("band", None, "dom", None, None),
        P(None, None, "dom", None, None),
        P("dom", None, None),
        P(),
        P("dom", None, None),
        P("dom"),
        P("dom"),
        P("dom"),
        P("dom"),
    )
    out_specs = (P("band", None, "dom", None, None), P(None, None, "dom"))
    return jax.shard_map(shards, mesh=mesh, in_specs=in_specs, out_specs=out_specs, check_vma=False)
```

```python
import jax
import jax.numpy as jnp
from jax import lax
from jax.sharding import PartitionSpec as P

STEPS = 2
TAYLOR = 4


spacing = 0.5
time_step = 0.04
highest = lax.Precision.HIGHEST


def extended_2(block, sides, width):
    for axis, dim in sides:
        count = lax.axis_size(axis)
        forward = [(i, i + 1) for i in range(count - 1)]
        backward = [(target, source) for source, target in forward]
        low = lax.ppermute(
            lax.slice_in_dim(block, block.shape[dim] - width, None, axis=dim), axis, forward
        )
        high = lax.ppermute(lax.slice_in_dim(block, 0, width, axis=dim), axis, backward)
        block = jnp.concatenate([low, block, high], axis=dim)
    return block


def laplace(extended):
    middle = extended[:, :, 2:-2]
    along_z = 16.0 * (extended[:, :, 3:-1] + extended[:, :, 1:-3]) - (
        extended[:, :, 4:] + extended[:, :, :-4]
    )
    along_x = 16.0 * (jnp.roll(middle, 1, 3) + jnp.roll(middle, -1, 3)) - (
        jnp.roll(middle, 2, 3) + jnp.roll(middle, -2, 3)
    )
    along_y = 16.0 * (jnp.roll(middle, 1, 4) + jnp.roll(middle, -1, 4)) - (
        jnp.roll(middle, 2, 4) + jnp.roll(middle, -2, 4)
    )
    return (along_z + along_x + along_y - 90.0 * middle) / (12.0 * spacing * spacing)


def projections(ace_rows, term):
    vector_count = ace_rows.shape[0]
    orbital_count = term.shape[0]
    products = lax.dot_general(
        ace_rows.reshape(vector_count * 2, -1),
        term.reshape(orbital_count * 2, -1),
        (((1,), (1,)), ((), ())),
        precision=highest,
        preferred_element_type=jnp.float32,
    )
    products = products.reshape(vector_count, 2, orbital_count, 2)
    return jnp.stack(
        [products[:, 0, :, 0] + products[:, 1, :, 1], products[:, 0, :, 1] - products[:, 1, :, 0]]
    )


def exchange_sum(x, axis):
    count = lax.axis_size(axis)
    copies = jnp.broadcast_to(x[None], (count,) + x.shape)
    return jnp.sum(lax.all_to_all(copies, axis, 0, 0, tiled=False), axis=0)


def ace_weights(ace_rows, term):
    return exchange_sum(projections(ace_rows, term), "dom")


def fock_term(ace_rows, weights):
    vector_count = ace_rows.shape[0]
    orbital_count = weights.shape[2]
    real_part = weights[0]
    imag_part = weights[1]
    coefficients = jnp.stack(
        [jnp.stack([real_part, imag_part], axis=-1), jnp.stack([-imag_part, real_part], axis=-1)],
        axis=1,
    )
    applied = lax.dot_general(
        coefficients.reshape(vector_count * 2, orbital_count * 2),
        ace_rows.reshape(vector_count * 2, -1),
        (((0,), (0,)), ((), ())),
        precision=highest,
        preferred_element_type=jnp.float32,
    )
    return applied.reshape((orbital_count, 2) + ace_rows.shape[2:])


def next_term(applied, degree):
    factor = time_step / degree
    return jnp.stack([factor * applied[:, 1], -factor * applied[:, 0]], axis=1)


def complex_product(left, right):
    real = jnp.einsum("km,mj->kj", left[0], right[0], precision=highest) - jnp.einsum(
        "km,mj->kj", left[1], right[1], precision=highest
    )
    imag = jnp.einsum("km,mj->kj", left[0], right[1], precision=highest) + jnp.einsum(
        "km,mj->kj", left[1], right[0], precision=highest
    )
    return jnp.stack([real, imag])


def kinetic_ace(ace_vectors, local_potential):
    extended = extended_2(ace_vectors, (("dom", 2),), 2)
    return -0.5 * laplace(extended) + local_potential * ace_vectors


def taylor_rounds(current, potential, ace_vectors, ace_applied, gram, gram_is_partial):
    accumulated = current
    term = current
    weights = None
    ahead = None
    for degree in range(1, TAYLOR + 1):
        if weights is None:
            pieces = [projections(ace_vectors, term), projections(ace_applied, term)]
            if gram_is_partial:
                pieces.append(gram)
            joined = exchange_sum(jnp.concatenate(pieces, axis=2), "dom")
            orbital_count = term.shape[0]
            weights = joined[:, :, :orbital_count]
            ahead = joined[:, :, orbital_count : 2 * orbital_count]
            if gram_is_partial:
                gram = joined[:, :, 2 * orbital_count :]
                gram_is_partial = False
        extended = extended_2(term, (("dom", 2),), 2)
        applied = -0.5 * laplace(extended) + potential * term - fock_term(ace_vectors, weights)
        if ahead is not None:
            factor = time_step / degree
            shifted = ahead - complex_product(gram, weights)
            weights = jnp.stack([factor * shifted[1], -factor * shifted[0]])
            ahead = None
        else:
            weights = None
        term = next_term(applied, degree)
        accumulated = accumulated + term
    return accumulated, gram


def projector_matrix(run_projectors, run_count, run_start, cell_count):
    slot_count, comp_count, point_count = run_projectors.shape
    lanes = 128
    tiles_out = cell_count // lanes
    span = point_count // lanes + 1
    points = jnp.arange(point_count, dtype=jnp.int32)
    masked = jnp.where(points[None, None, :] < run_count[:, None, None], run_projectors, 0.0)
    window = jnp.pad(masked, ((0, 0), (0, 0), (0, span * lanes - point_count)))
    shift = run_start % lanes
    amount = 1
    while amount < lanes:
        moved = jnp.pad(window[:, :, : window.shape[2] - amount], ((0, 0), (0, 0), (amount, 0)))
        window = jnp.where(((shift // amount) % 2 == 1)[:, None, None], moved, window)
        amount *= 2
    window = window.reshape(slot_count, comp_count, span, lanes)
    first_tile = run_start // lanes
    tile_ids = jnp.arange(tiles_out, dtype=jnp.int32)
    full = jnp.zeros((slot_count, comp_count, tiles_out, lanes), jnp.float32)
    for offset in range(span):
        hit = (tile_ids[None, :] == (first_tile + offset)[:, None])[:, None, :, None]
        full = full + jnp.where(hit, window[:, :, offset][:, :, None, :], 0.0)
    return full.reshape(slot_count * comp_count, cell_count)


def run_partials(current, matrix, slot_count):
    flattened = current.reshape(current.shape[0] * 2, -1)
    products = jnp.einsum("kn,rn->kr", matrix, flattened, precision=highest)
    return products.reshape(slot_count, -1, flattened.shape[0])


def atom_forces(partials, run_atom, kb_energy):
    atom_dev = kb_energy.shape[0]
    dom_count = lax.axis_size("dom")
    slot_count = run_atom.shape[0]
    capacity = 2 * slot_count // dom_count
    owner = run_atom // atom_dev
    slot_ids = jnp.arange(slot_count, dtype=jnp.int32)
    same_owner = (owner[:, None] == owner[None, :]) & (slot_ids[None, :] < slot_ids[:, None])
    owner_rank = jnp.sum(same_owner.astype(jnp.int32), axis=1)
    slot_pos = owner * capacity + owner_rank
    placement = jnp.arange(dom_count * capacity, dtype=jnp.int32)[:, None] == slot_pos[None, :]
    outgoing = jnp.einsum("ks,stcr->ktcr", placement.astype(jnp.float32), partials, precision=highest)
    atom_slots = jnp.max(jnp.where(placement, (run_atom % atom_dev)[None, :], -1), axis=1)
    received, received_ids = (
        lax.all_to_all(outgoing, "dom", split_axis=0, concat_axis=0, tiled=True),
        lax.all_to_all(atom_slots, "dom", split_axis=0, concat_axis=0, tiled=True),
    )
    matches = (received_ids[None, :] == jnp.arange(atom_dev, dtype=jnp.int32)[:, None]).astype(
        jnp.float32
    )
    atom_totals = jnp.einsum("ak,ktcr->atcr", matches, received, precision=highest)
    return (
        2.0
        * kb_energy[None, None, :]
        * jnp.einsum("atr,atcr->tca", atom_totals[:, :, 0], atom_totals[:, :, 1:], precision=highest)
    )


def shards(
    orbitals,
    ace_vectors,
    local_potential,
    field_strength,
    run_projectors,
    run_atom,
    run_count,
    run_start,
    kb_energy,
):
    plane_count = orbitals.shape[2]
    plane_total = plane_count * lax.axis_size("dom")
    first_plane = lax.axis_index("dom") * plane_count
    height = (
        2.0
        * ((first_plane + jnp.arange(plane_count, dtype=jnp.int32)).astype(jnp.float32) + 0.5)
        / plane_total
        - 1.0
    )
    slot_count = run_projectors.shape[0]
    cell_count = orbitals[0, 0].size
    matrix = projector_matrix(run_projectors, run_count, run_start, cell_count)
    current = orbitals
    results = []
    ace_kinetic = kinetic_ace(ace_vectors, local_potential)
    ace_height = height[:, None, None] * ace_vectors
    gram = projections(ace_vectors, ace_vectors)
    for step_index in range(STEPS):
        strength = field_strength[step_index]
        current, gram = taylor_rounds(
            current,
            local_potential + strength * height[:, None, None],
            ace_vectors,
            ace_kinetic + strength * ace_height,
            gram,
            step_index == 0,
        )
        results.append(run_partials(current, matrix, slot_count))
    partials = jnp.stack(results, axis=1)
    forces = exchange_sum(atom_forces(partials, run_atom, kb_energy), "band")
    return (current, forces)


def solution(mesh):
    in_specs = (
        P("band", None, "dom", None, None),
        P(None, None, "dom", None, None),
        P("dom", None, None),
        P(),
        P("dom", None, None),
        P("dom"),
        P("dom"),
        P("dom"),
        P("dom"),
    )
    out_specs = (P("band", None, "dom", None, None), P(None, None, "dom"))
    return jax.shard_map(shards, mesh=mesh, in_specs=in_specs, out_specs=out_specs, check_vma=False)
```

```python
import jax
import jax.numpy as jnp
from jax import lax
from jax.sharding import PartitionSpec as P

STEPS = 2
TAYLOR = 4


spacing = 0.5
time_step = 0.04
highest = lax.Precision.HIGHEST


def extended_2(block, sides, width):
    for axis, dim in sides:
        count = lax.axis_size(axis)
        forward = [(i, i + 1) for i in range(count - 1)]
        backward = [(target, source) for source, target in forward]
        low = lax.ppermute(
            lax.slice_in_dim(block, block.shape[dim] - width, None, axis=dim), axis, forward
        )
        high = lax.ppermute(lax.slice_in_dim(block, 0, width, axis=dim), axis, backward)
        block = jnp.concatenate([low, block, high], axis=dim)
    return block


def laplace(extended):
    middle = extended[:, :, 2:-2]
    along_z = 16.0 * (extended[:, :, 3:-1] + extended[:, :, 1:-3]) - (
        extended[:, :, 4:] + extended[:, :, :-4]
    )
    along_x = 16.0 * (jnp.roll(middle, 1, 3) + jnp.roll(middle, -1, 3)) - (
        jnp.roll(middle, 2, 3) + jnp.roll(middle, -2, 3)
    )
    along_y = 16.0 * (jnp.roll(middle, 1, 4) + jnp.roll(middle, -1, 4)) - (
        jnp.roll(middle, 2, 4) + jnp.roll(middle, -2, 4)
    )
    return (along_z + along_x + along_y - 90.0 * middle) / (12.0 * spacing * spacing)


def projections(ace_rows, term):
    vector_count = ace_rows.shape[0]
    orbital_count = term.shape[0]
    products = lax.dot_general(
        ace_rows.reshape(vector_count * 2, -1),
        term.reshape(orbital_count * 2, -1),
        (((1,), (1,)), ((), ())),
        precision=highest,
        preferred_element_type=jnp.float32,
    )
    products = products.reshape(vector_count, 2, orbital_count, 2)
    return jnp.stack(
        [products[:, 0, :, 0] + products[:, 1, :, 1], products[:, 0, :, 1] - products[:, 1, :, 0]]
    )


def exchange_sum(x, axis):
    count = lax.axis_size(axis)
    copies = jnp.broadcast_to(x[None], (count,) + x.shape)
    return jnp.sum(lax.all_to_all(copies, axis, 0, 0, tiled=False), axis=0)


def ace_weights(ace_rows, term):
    return exchange_sum(projections(ace_rows, term), "dom")


def fock_term(ace_rows, weights):
    vector_count = ace_rows.shape[0]
    orbital_count = weights.shape[2]
    real_part = weights[0]
    imag_part = weights[1]
    coefficients = jnp.stack(
        [jnp.stack([real_part, imag_part], axis=-1), jnp.stack([-imag_part, real_part], axis=-1)],
        axis=1,
    )
    applied = lax.dot_general(
        coefficients.reshape(vector_count * 2, orbital_count * 2),
        ace_rows.reshape(vector_count * 2, -1),
        (((0,), (0,)), ((), ())),
        precision=highest,
        preferred_element_type=jnp.float32,
    )
    return applied.reshape((orbital_count, 2) + ace_rows.shape[2:])


def next_term(applied, degree):
    factor = time_step / degree
    return jnp.stack([factor * applied[:, 1], -factor * applied[:, 0]], axis=1)


def complex_product(left, right):
    real = jnp.einsum("km,mj->kj", left[0], right[0], precision=highest) - jnp.einsum(
        "km,mj->kj", left[1], right[1], precision=highest
    )
    imag = jnp.einsum("km,mj->kj", left[0], right[1], precision=highest) + jnp.einsum(
        "km,mj->kj", left[1], right[0], precision=highest
    )
    return jnp.stack([real, imag])


def taylor_rounds(current, potential, ace_vectors, gram, gram_is_partial):
    accumulated = current
    term = current
    weights = None
    orbital_count = current.shape[0]
    for degree in range(1, TAYLOR + 1):
        extended = extended_2(term, (("dom", 2),), 2)
        kinetic = -0.5 * laplace(extended) + potential * term
        ahead = None
        if weights is None:
            pieces = [projections(ace_vectors, term), projections(ace_vectors, kinetic)]
            if gram_is_partial:
                pieces.append(gram)
            joined = exchange_sum(jnp.concatenate(pieces, axis=2), "dom")
            weights = joined[:, :, :orbital_count]
            ahead = joined[:, :, orbital_count : 2 * orbital_count]
            if gram_is_partial:
                gram = joined[:, :, 2 * orbital_count :]
                gram_is_partial = False
        applied = kinetic - fock_term(ace_vectors, weights)
        if ahead is not None:
            factor = time_step / degree
            shifted = ahead - complex_product(gram, weights)
            weights = jnp.stack([factor * shifted[1], -factor * shifted[0]])
        else:
            weights = None
        term = next_term(applied, degree)
        accumulated = accumulated + term
    return accumulated, gram


def projector_matrix(run_projectors, run_count, run_start, cell_count):
    slot_count, comp_count, point_count = run_projectors.shape
    lanes = 128
    tiles_out = cell_count // lanes
    span = point_count // lanes + 1
    points = jnp.arange(point_count, dtype=jnp.int32)
    masked = jnp.where(points[None, None, :] < run_count[:, None, None], run_projectors, 0.0)
    window = jnp.pad(masked, ((0, 0), (0, 0), (0, span * lanes - point_count)))
    shift = run_start % lanes
    amount = 1
    while amount < lanes:
        moved = jnp.pad(window[:, :, : window.shape[2] - amount], ((0, 0), (0, 0), (amount, 0)))
        window = jnp.where(((shift // amount) % 2 == 1)[:, None, None], moved, window)
        amount *= 2
    window = window.reshape(slot_count, comp_count, span, lanes)
    first_tile = run_start // lanes
    tile_ids = jnp.arange(tiles_out, dtype=jnp.int32)
    full = jnp.zeros((slot_count, comp_count, tiles_out, lanes), jnp.float32)
    for offset in range(span):
        hit = (tile_ids[None, :] == (first_tile + offset)[:, None])[:, None, :, None]
        full = full + jnp.where(hit, window[:, :, offset][:, :, None, :], 0.0)
    return full.reshape(slot_count * comp_count, cell_count)


def run_partials(current, matrix, slot_count):
    flattened = current.reshape(current.shape[0] * 2, -1)
    products = jnp.einsum("kn,rn->kr", matrix, flattened, precision=highest)
    return products.reshape(slot_count, -1, flattened.shape[0])


def atom_forces(partials, run_atom, kb_energy):
    atom_dev = kb_energy.shape[0]
    dom_count = lax.axis_size("dom")
    slot_count = run_atom.shape[0]
    capacity = 2 * slot_count // dom_count
    owner = run_atom // atom_dev
    slot_ids = jnp.arange(slot_count, dtype=jnp.int32)
    same_owner = (owner[:, None] == owner[None, :]) & (slot_ids[None, :] < slot_ids[:, None])
    owner_rank = jnp.sum(same_owner.astype(jnp.int32), axis=1)
    slot_pos = owner * capacity + owner_rank
    placement = jnp.arange(dom_count * capacity, dtype=jnp.int32)[:, None] == slot_pos[None, :]
    outgoing = jnp.einsum("ks,stcr->ktcr", placement.astype(jnp.float32), partials, precision=highest)
    atom_slots = jnp.max(jnp.where(placement, (run_atom % atom_dev)[None, :], -1), axis=1)
    received, received_ids = (
        lax.all_to_all(outgoing, "dom", split_axis=0, concat_axis=0, tiled=True),
        lax.all_to_all(atom_slots, "dom", split_axis=0, concat_axis=0, tiled=True),
    )
    matches = (received_ids[None, :] == jnp.arange(atom_dev, dtype=jnp.int32)[:, None]).astype(
        jnp.float32
    )
    atom_totals = jnp.einsum("ak,ktcr->atcr", matches, received, precision=highest)
    return (
        2.0
        * kb_energy[None, None, :]
        * jnp.einsum("atr,atcr->tca", atom_totals[:, :, 0], atom_totals[:, :, 1:], precision=highest)
    )


def shards(
    orbitals,
    ace_vectors,
    local_potential,
    field_strength,
    run_projectors,
    run_atom,
    run_count,
    run_start,
    kb_energy,
):
    plane_count = orbitals.shape[2]
    plane_total = plane_count * lax.axis_size("dom")
    first_plane = lax.axis_index("dom") * plane_count
    height = (
        2.0
        * ((first_plane + jnp.arange(plane_count, dtype=jnp.int32)).astype(jnp.float32) + 0.5)
        / plane_total
        - 1.0
    )
    slot_count = run_projectors.shape[0]
    cell_count = orbitals[0, 0].size
    matrix = projector_matrix(run_projectors, run_count, run_start, cell_count)
    current = orbitals
    results = []
    gram = projections(ace_vectors, ace_vectors)
    for step_index in range(STEPS):
        strength = field_strength[step_index]
        current, gram = taylor_rounds(
            current,
            local_potential + strength * height[:, None, None],
            ace_vectors,
            gram,
            step_index == 0,
        )
        results.append(run_partials(current, matrix, slot_count))
    partials = jnp.stack(results, axis=1)
    forces = exchange_sum(atom_forces(partials, run_atom, kb_energy), "band")
    return (current, forces)


def solution(mesh):
    in_specs = (
        P("band", None, "dom", None, None),
        P(None, None, "dom", None, None),
        P("dom", None, None),
        P(),
        P("dom", None, None),
        P("dom"),
        P("dom"),
        P("dom"),
        P("dom"),
    )
    out_specs = (P("band", None, "dom", None, None), P(None, None, "dom"))
    return jax.shard_map(shards, mesh=mesh, in_specs=in_specs, out_specs=out_specs, check_vma=False)
```

```python
import jax
import jax.numpy as jnp
from jax import lax
from jax.sharding import PartitionSpec as P

STEPS = 2
TAYLOR = 4


spacing = 0.5
time_step = 0.04
highest = lax.Precision.HIGHEST


def extended_2(block, sides, width):
    for axis, dim in sides:
        count = lax.axis_size(axis)
        forward = [(i, i + 1) for i in range(count - 1)]
        backward = [(target, source) for source, target in forward]
        low = lax.ppermute(
            lax.slice_in_dim(block, block.shape[dim] - width, None, axis=dim), axis, forward
        )
        high = lax.ppermute(lax.slice_in_dim(block, 0, width, axis=dim), axis, backward)
        block = jnp.concatenate([low, block, high], axis=dim)
    return block


def laplace(extended):
    middle = extended[:, :, 2:-2]
    along_z = 16.0 * (extended[:, :, 3:-1] + extended[:, :, 1:-3]) - (
        extended[:, :, 4:] + extended[:, :, :-4]
    )
    along_x = 16.0 * (jnp.roll(middle, 1, 3) + jnp.roll(middle, -1, 3)) - (
        jnp.roll(middle, 2, 3) + jnp.roll(middle, -2, 3)
    )
    along_y = 16.0 * (jnp.roll(middle, 1, 4) + jnp.roll(middle, -1, 4)) - (
        jnp.roll(middle, 2, 4) + jnp.roll(middle, -2, 4)
    )
    return (along_z + along_x + along_y - 90.0 * middle) / (12.0 * spacing * spacing)


def projections(ace_rows, term):
    vector_count = ace_rows.shape[0]
    orbital_count = term.shape[0]
    products = lax.dot_general(
        ace_rows.reshape(vector_count * 2, -1),
        term.reshape(orbital_count * 2, -1),
        (((1,), (1,)), ((), ())),
        precision=highest,
        preferred_element_type=jnp.float32,
    )
    products = products.reshape(vector_count, 2, orbital_count, 2)
    return jnp.stack(
        [products[:, 0, :, 0] + products[:, 1, :, 1], products[:, 0, :, 1] - products[:, 1, :, 0]]
    )


def exchange_sum(x, axis):
    count = lax.axis_size(axis)
    copies = jnp.broadcast_to(x[None], (count,) + x.shape)
    return jnp.sum(lax.all_to_all(copies, axis, 0, 0, tiled=False), axis=0)


def ace_weights(ace_rows, term):
    return exchange_sum(projections(ace_rows, term), "dom")


def fock_term(ace_rows, weights):
    vector_count = ace_rows.shape[0]
    orbital_count = weights.shape[2]
    real_part = weights[0]
    imag_part = weights[1]
    coefficients = jnp.stack(
        [jnp.stack([real_part, imag_part], axis=-1), jnp.stack([-imag_part, real_part], axis=-1)],
        axis=1,
    )
    applied = lax.dot_general(
        coefficients.reshape(vector_count * 2, orbital_count * 2),
        ace_rows.reshape(vector_count * 2, -1),
        (((0,), (0,)), ((), ())),
        precision=highest,
        preferred_element_type=jnp.float32,
    )
    return applied.reshape((orbital_count, 2) + ace_rows.shape[2:])


def next_term(applied, degree):
    factor = time_step / degree
    return jnp.stack([factor * applied[:, 1], -factor * applied[:, 0]], axis=1)


def complex_product(left, right):
    real = jnp.einsum("km,mj->kj", left[0], right[0], precision=highest) - jnp.einsum(
        "km,mj->kj", left[1], right[1], precision=highest
    )
    imag = jnp.einsum("km,mj->kj", left[0], right[1], precision=highest) + jnp.einsum(
        "km,mj->kj", left[1], right[0], precision=highest
    )
    return jnp.stack([real, imag])


def taylor_rounds(current, potential, ace_vectors, gram, gram_is_partial):
    accumulated = current
    term = current
    weights = None
    orbital_count = current.shape[0]
    for degree in range(1, TAYLOR + 1):
        extended = extended_2(term, (("dom", 2),), 2)
        kinetic = -0.5 * laplace(extended) + potential * term
        ahead = None
        if weights is None:
            pieces = [projections(ace_vectors, term), projections(ace_vectors, kinetic)]
            if gram_is_partial:
                pieces.append(gram)
            joined = exchange_sum(jnp.concatenate(pieces, axis=2), "dom")
            weights = joined[:, :, :orbital_count]
            ahead = joined[:, :, orbital_count : 2 * orbital_count]
            if gram_is_partial:
                gram = joined[:, :, 2 * orbital_count :]
                gram_is_partial = False
        applied = kinetic - fock_term(ace_vectors, weights)
        if ahead is not None:
            factor = time_step / degree
            shifted = ahead - complex_product(gram, weights)
            weights = jnp.stack([factor * shifted[1], -factor * shifted[0]])
        else:
            weights = None
        term = next_term(applied, degree)
        accumulated = accumulated + term
    return accumulated, gram


def projector_matrix(run_projectors, run_count, run_start, cell_count):
    slot_count, comp_count, point_count = run_projectors.shape
    lanes = 128
    tiles_out = cell_count // lanes
    span = point_count // lanes + 1
    points = jnp.arange(point_count, dtype=jnp.int32)
    masked = jnp.where(points[None, None, :] < run_count[:, None, None], run_projectors, 0.0)
    window = jnp.pad(masked, ((0, 0), (0, 0), (0, span * lanes - point_count)))
    shift = run_start % lanes
    amount = 1
    while amount < lanes:
        moved = jnp.pad(window[:, :, : window.shape[2] - amount], ((0, 0), (0, 0), (amount, 0)))
        window = jnp.where(((shift // amount) % 2 == 1)[:, None, None], moved, window)
        amount *= 2
    window = window.reshape(slot_count, comp_count, span, lanes)
    first_tile = run_start // lanes
    tile_ids = jnp.arange(tiles_out, dtype=jnp.int32)
    full = jnp.zeros((slot_count, comp_count, tiles_out, lanes), jnp.float32)
    for offset in range(span):
        hit = (tile_ids[None, :] == (first_tile + offset)[:, None])[:, None, :, None]
        full = full + jnp.where(hit, window[:, :, offset][:, :, None, :], 0.0)
    return full.reshape(slot_count * comp_count, cell_count)


def run_partials(states, matrix, slot_count):
    step_count = states.shape[0]
    flattened = states.reshape(step_count * states.shape[1] * 2, -1)
    products = jnp.einsum("kn,rn->kr", matrix, flattened, precision=highest)
    products = products.reshape(slot_count, -1, step_count, flattened.shape[0] // step_count)
    return jnp.transpose(products, (0, 2, 1, 3))


def atom_forces(partials, run_atom, kb_energy):
    atom_dev = kb_energy.shape[0]
    dom_count = lax.axis_size("dom")
    atom_ids = jnp.arange(dom_count * atom_dev, dtype=jnp.int32)
    owned = (run_atom[None, :] == atom_ids[:, None]).astype(jnp.float32)
    outgoing = jnp.einsum("as,stcr->atcr", owned, partials, precision=highest)
    received = lax.all_to_all(outgoing, "dom", split_axis=0, concat_axis=0, tiled=True)
    atom_totals = jnp.sum(received.reshape((dom_count, atom_dev) + received.shape[1:]), axis=0)
    return (
        2.0
        * kb_energy[None, None, :]
        * jnp.einsum("atr,atcr->tca", atom_totals[:, :, 0], atom_totals[:, :, 1:], precision=highest)
    )


def shards(
    orbitals,
    ace_vectors,
    local_potential,
    field_strength,
    run_projectors,
    run_atom,
    run_count,
    run_start,
    kb_energy,
):
    plane_count = orbitals.shape[2]
    plane_total = plane_count * lax.axis_size("dom")
    first_plane = lax.axis_index("dom") * plane_count
    height = (
        2.0
        * ((first_plane + jnp.arange(plane_count, dtype=jnp.int32)).astype(jnp.float32) + 0.5)
        / plane_total
        - 1.0
    )
    slot_count = run_projectors.shape[0]
    cell_count = orbitals[0, 0].size
    matrix = projector_matrix(run_projectors, run_count, run_start, cell_count)
    current = orbitals
    states = []
    gram = projections(ace_vectors, ace_vectors)
    for step_index in range(STEPS):
        strength = field_strength[step_index]
        current, gram = taylor_rounds(
            current,
            local_potential + strength * height[:, None, None],
            ace_vectors,
            gram,
            step_index == 0,
        )
        states.append(current)
    partials = run_partials(jnp.stack(states), matrix, slot_count)
    forces = exchange_sum(atom_forces(partials, run_atom, kb_energy), "band")
    return (current, forces)


def solution(mesh):
    in_specs = (
        P("band", None, "dom", None, None),
        P(None, None, "dom", None, None),
        P("dom", None, None),
        P(),
        P("dom", None, None),
        P("dom"),
        P("dom"),
        P("dom"),
        P("dom"),
    )
    out_specs = (P("band", None, "dom", None, None), P(None, None, "dom"))
    return jax.shard_map(shards, mesh=mesh, in_specs=in_specs, out_specs=out_specs, check_vma=False)
```

```python
import jax
import jax.numpy as jnp
from jax import lax
from jax.sharding import PartitionSpec as P

STEPS = 2
TAYLOR = 4


spacing = 0.5
time_step = 0.04
highest = lax.Precision.HIGHEST


def extended_2(block, sides, width):
    for axis, dim in sides:
        count = lax.axis_size(axis)
        forward = [(i, i + 1) for i in range(count - 1)]
        backward = [(target, source) for source, target in forward]
        low = lax.ppermute(
            lax.slice_in_dim(block, block.shape[dim] - width, None, axis=dim), axis, forward
        )
        high = lax.ppermute(lax.slice_in_dim(block, 0, width, axis=dim), axis, backward)
        block = jnp.concatenate([low, block, high], axis=dim)
    return block


def laplace(extended):
    middle = extended[:, :, 2:-2]
    along_z = 16.0 * (extended[:, :, 3:-1] + extended[:, :, 1:-3]) - (
        extended[:, :, 4:] + extended[:, :, :-4]
    )
    along_x = 16.0 * (jnp.roll(middle, 1, 3) + jnp.roll(middle, -1, 3)) - (
        jnp.roll(middle, 2, 3) + jnp.roll(middle, -2, 3)
    )
    along_y = 16.0 * (jnp.roll(middle, 1, 4) + jnp.roll(middle, -1, 4)) - (
        jnp.roll(middle, 2, 4) + jnp.roll(middle, -2, 4)
    )
    return (along_z + along_x + along_y - 90.0 * middle) / (12.0 * spacing * spacing)


def projections(ace_rows, term):
    vector_count = ace_rows.shape[0]
    orbital_count = term.shape[0]
    products = lax.dot_general(
        ace_rows.reshape(vector_count * 2, -1),
        term.reshape(orbital_count * 2, -1),
        (((1,), (1,)), ((), ())),
        precision=highest,
        preferred_element_type=jnp.float32,
    )
    products = products.reshape(vector_count, 2, orbital_count, 2)
    return jnp.stack(
        [products[:, 0, :, 0] + products[:, 1, :, 1], products[:, 0, :, 1] - products[:, 1, :, 0]]
    )


def exchange_sum(x, axis):
    count = lax.axis_size(axis)
    copies = jnp.broadcast_to(x[None], (count,) + x.shape)
    return jnp.sum(lax.all_to_all(copies, axis, 0, 0, tiled=False), axis=0)


def ace_weights(ace_rows, term):
    return exchange_sum(projections(ace_rows, term), "dom")


def fock_term(ace_rows, weights):
    vector_count = ace_rows.shape[0]
    orbital_count = weights.shape[2]
    real_part = weights[0]
    imag_part = weights[1]
    coefficients = jnp.stack(
        [jnp.stack([real_part, imag_part], axis=-1), jnp.stack([-imag_part, real_part], axis=-1)],
        axis=1,
    )
    applied = lax.dot_general(
        coefficients.reshape(vector_count * 2, orbital_count * 2),
        ace_rows.reshape(vector_count * 2, -1),
        (((0,), (0,)), ((), ())),
        precision=highest,
        preferred_element_type=jnp.float32,
    )
    return applied.reshape((orbital_count, 2) + ace_rows.shape[2:])


def next_term(applied, degree):
    factor = time_step / degree
    return jnp.stack([factor * applied[:, 1], -factor * applied[:, 0]], axis=1)


def complex_product(left, right):
    real = jnp.einsum("km,mj->kj", left[0], right[0], precision=highest) - jnp.einsum(
        "km,mj->kj", left[1], right[1], precision=highest
    )
    imag = jnp.einsum("km,mj->kj", left[0], right[1], precision=highest) + jnp.einsum(
        "km,mj->kj", left[1], right[0], precision=highest
    )
    return jnp.stack([real, imag])


def taylor_rounds(current, potential, ace_vectors, gram, gram_is_partial):
    accumulated = current
    term = current
    weights = None
    orbital_count = current.shape[0]
    for degree in range(1, TAYLOR + 1):
        extended = extended_2(term, (("dom", 2),), 2)
        kinetic = -0.5 * laplace(extended) + potential * term
        ahead = None
        if weights is None:
            pieces = [projections(ace_vectors, term), projections(ace_vectors, kinetic)]
            if gram_is_partial:
                pieces.append(gram)
            joined = exchange_sum(jnp.concatenate(pieces, axis=2), "dom")
            weights = joined[:, :, :orbital_count]
            ahead = joined[:, :, orbital_count : 2 * orbital_count]
            if gram_is_partial:
                gram = joined[:, :, 2 * orbital_count :]
                gram_is_partial = False
        applied = kinetic - fock_term(ace_vectors, weights)
        if ahead is not None:
            factor = time_step / degree
            shifted = ahead - complex_product(gram, weights)
            weights = jnp.stack([factor * shifted[1], -factor * shifted[0]])
        else:
            weights = None
        term = next_term(applied, degree)
        accumulated = accumulated + term
    return accumulated, gram


def projector_matrix(run_projectors, run_count, run_start, cell_count):
    slot_count, comp_count, point_count = run_projectors.shape
    lanes = 128
    tiles_out = cell_count // lanes
    span = point_count // lanes + 1
    points = jnp.arange(point_count, dtype=jnp.int32)
    masked = jnp.where(points[None, None, :] < run_count[:, None, None], run_projectors, 0.0)
    window = jnp.pad(masked, ((0, 0), (0, 0), (0, span * lanes - point_count)))
    shift = run_start % lanes
    amount = 1
    while amount < lanes:
        moved = jnp.pad(window[:, :, : window.shape[2] - amount], ((0, 0), (0, 0), (amount, 0)))
        window = jnp.where(((shift // amount) % 2 == 1)[:, None, None], moved, window)
        amount *= 2
    window = window.reshape(slot_count, comp_count, span, lanes)
    first_tile = run_start // lanes
    tile_ids = jnp.arange(tiles_out, dtype=jnp.int32)
    full = jnp.zeros((slot_count, comp_count, tiles_out, lanes), jnp.float32)
    for offset in range(span):
        hit = (tile_ids[None, :] == (first_tile + offset)[:, None])[:, None, :, None]
        full = full + jnp.where(hit, window[:, :, offset][:, :, None, :], 0.0)
    return full.reshape(slot_count * comp_count, cell_count)


def run_partials(current, matrix, slot_count):
    flattened = current.reshape(current.shape[0] * 2, -1)
    products = jnp.einsum("kn,rn->kr", matrix, flattened, precision=highest)
    return products.reshape(slot_count, -1, flattened.shape[0])


def atom_forces(partials, run_atom, kb_energy):
    atom_dev = kb_energy.shape[0]
    dom_count = lax.axis_size("dom")
    atom_ids = jnp.arange(dom_count * atom_dev, dtype=jnp.int32)
    owned = (run_atom[None, :] == atom_ids[:, None]).astype(jnp.float32)
    outgoing = jnp.einsum("as,stcr->atcr", owned, partials, precision=highest)
    received = lax.all_to_all(outgoing, "dom", split_axis=0, concat_axis=0, tiled=True)
    atom_totals = jnp.sum(received.reshape((dom_count, atom_dev) + received.shape[1:]), axis=0)
    return (
        2.0
        * kb_energy[None, None, :]
        * jnp.einsum("atr,atcr->tca", atom_totals[:, :, 0], atom_totals[:, :, 1:], precision=highest)
    )


def shards(
    orbitals,
    ace_vectors,
    local_potential,
    field_strength,
    run_projectors,
    run_atom,
    run_count,
    run_start,
    kb_energy,
):
    plane_count = orbitals.shape[2]
    plane_total = plane_count * lax.axis_size("dom")
    first_plane = lax.axis_index("dom") * plane_count
    height = (
        2.0
        * ((first_plane + jnp.arange(plane_count, dtype=jnp.int32)).astype(jnp.float32) + 0.5)
        / plane_total
        - 1.0
    )
    slot_count = run_projectors.shape[0]
    cell_count = orbitals[0, 0].size
    matrix = projector_matrix(run_projectors, run_count, run_start, cell_count)
    current = orbitals
    results = []
    gram = projections(ace_vectors, ace_vectors)
    for step_index in range(STEPS):
        strength = field_strength[step_index]
        current, gram = taylor_rounds(
            current,
            local_potential + strength * height[:, None, None],
            ace_vectors,
            gram,
            step_index == 0,
        )
        results.append(run_partials(current, matrix, slot_count))
    partials = jnp.stack(results, axis=1)
    forces = exchange_sum(atom_forces(partials, run_atom, kb_energy), "band")
    return (current, forces)


def solution(mesh):
    in_specs = (
        P("band", None, "dom", None, None),
        P(None, None, "dom", None, None),
        P("dom", None, None),
        P(),
        P("dom", None, None),
        P("dom"),
        P("dom"),
        P("dom"),
        P("dom"),
    )
    out_specs = (P("band", None, "dom", None, None), P(None, None, "dom"))
    return jax.shard_map(shards, mesh=mesh, in_specs=in_specs, out_specs=out_specs, check_vma=False)
```
